512 devices in a mesh: section: 8 (over y), dp: 64 (over x, z, core).
Axes of the slice: x: 4, y: 8, z: 8, core: 2. Of those that a mesh axis runs over, the one named last changes fastest.
Arguments:
- queries: bfloat16 [65536, 3584], P(('section', 'dp')), may hold values from -1 to 1
- passages: bfloat16 [128, 64, 3584], P('dp'), may hold values from -1 to 1
- candidates: int32 [512, 3], P('section'), may hold values from 0 to 63, as said below
- counts: int32 [512], P('section'), may hold values from 1 to 3, 1024 in all
- teacher: float32 [65536, 384], P(('section', 'dp')), may hold values from -20 to 450
- section_weights: bfloat16 [8, 3584, 3584], P('section', 'dp'), may hold values from -0.09375 to 0.09375
- section_inputs: bfloat16 [8, 64, 3584], P('section', None, 'dp'), may hold values from -1.5 to 1.5
- pre_acts: bfloat16 [8, 64, 3584], P('section', None, 'dp'), may hold values from -8 to 8
Outputs:
- query_grads: bfloat16 [65536, 3584], P(('section', 'dp'))
- passage_grads: bfloat16 [128, 64, 3584], P('dp')
- grad_inputs: float32 [8, 64, 3584], P('section', None, 'dp')
- weight_grads: bfloat16 [8, 3584, 3584], P('section', 'dp')
The draws below stay inside these ranges and needn't reach their ends.
Inputs may be any that keep to these rules, and one draw needn't show every extreme that they name: `candidates`: each row names 3 different passage blocks. A query block uses the first counts[b] entries of its row of candidates.
All inputs are finite; a program needn't handle non-finite values.
Results may differ from the reference program's by a relative error of at most 0.0085.
Values may be sent and summed in bfloat16 or wider, within the bound.
No kernel may reach another device: no remote copies, remote signals or barrier semaphores. Data moves between devices by JAX's collectives and lax.ppermute only.
A program may use at most 64 MiB of HBM per device.

```python
import math
import jax
import jax.numpy as jnp
import numpy as np
from jax import lax

D = 3584
BLOCK = 128
C_MAX = 3
QB_DEV = 1
MB_DEV = 1
NQB = 512
NQ = 65536
NPB = 64
M = 64
N_SECTION = 8
N_DP = 64


def embed_scale():
    return 0.387 * float(D) ** (-0.25)


def passage_row(key, row_pos, block_pos):
    inner_key = jax.random.fold_in(jax.random.fold_in(jax.random.fold_in(key, 301), row_pos), block_pos)
    return jax.random.truncated_normal(inner_key, -6.0, 6.0, (D,), jnp.float32) * embed_scale()


def row_block_count(key, row_pos):
    blocks = jnp.arange(NPB, dtype=jnp.int32)
    return jax.vmap(lambda block_pos: passage_row(key, row_pos, block_pos))(blocks)


def passage_table(key):
    rows = jnp.arange(BLOCK, dtype=jnp.int32)
    return jax.vmap(lambda row_pos: row_block_count(key, row_pos))(rows)


def candidate_table(key):
    weight_matrices = jax.random.randint(jax.random.fold_in(key, 401), (NPB,), 1, 5)
    draws = jax.random.randint(jax.random.fold_in(key, 402), (NQB, NPB), 0, 4096)
    ranks = jnp.arange(NPB, dtype=jnp.int32)
    row_ids = jnp.arange(NQB, dtype=jnp.int32)[:, None]
    scores = draws * weight_matrices[None, :] * NPB + ranks[None, :]
    scores = scores + jnp.where((row_ids == 0) & (ranks[None, :] == NPB - 1), 1 << 29, 0)
    scores = scores + jnp.where((row_ids == 1) & (ranks[None, :] == 0), 1 << 29, 0)
    return lax.top_k(scores, C_MAX)[1].astype(jnp.int32)


def draw_candidates(key, part):
    return candidate_table(key)


def draw_passages(key, part):
    table = passage_table(key)
    return jnp.clip(table, -1.0, 1.0).astype(jnp.bfloat16)


def draw_queries(key, part):
    values = jax.random.truncated_normal(jax.random.fold_in(key, 601), -6.0, 6.0, (NQ, D), jnp.float32)
    values = values * embed_scale()
    return jnp.clip(values, -1.0, 1.0).astype(jnp.bfloat16)


def draw_teacher(key, part):
    values = jax.random.truncated_normal(jax.random.fold_in(key, 703), -6.0, 6.0, (NQ, C_MAX * BLOCK), jnp.float32) * 3.0
    return values.astype(jnp.float32)


def level_of(key, extent, split, least, largest):
    factor_of, own = 1.0, jax.random.fold_in(key, 6)
    for axis_at, blocks in split:
        steps = jnp.exp(jax.random.uniform(jax.random.fold_in(own, axis_at), (blocks,), jnp.float32, least / len(split), largest / len(split)))
        factor_of = factor_of * jnp.repeat(steps, extent[axis_at] // blocks).reshape([-1 if axis == axis_at else 1 for axis in range(len(extent))])
    return factor_of


def length_profile(amount, total, limit, skew):
    loads = [(1 << 20) // math.isqrt(rank ** skew) + 1 for rank in range(2, amount + 1)]
    surplus, given = total - limit - (amount - 1), [1] * (amount - 1)
    while surplus > 0:
        free = [i for i in range(amount - 1) if given[i] < limit]
        mass, budget = sum([loads[i] for i in free]), surplus
        for i in free:
            more = min(limit - given[i], max(1, budget * loads[i] // mass), surplus)
            given[i] = given[i] + more
            surplus = surplus - more
    return np.array([limit] + given)


def ragged(key, amount, total, reach, slope):
    if amount == 2:
        one = jax.random.randint(key, (), max(1, total - reach), min(reach, total - 1) + 1)
        return jnp.stack([one, total - one])
    sizes = jnp.asarray(length_profile(amount, total, reach, slope), jnp.int32)
    couples = (amount - 1) // 2
    giver, sink = sizes[1:1 + 2 * couples:2], sizes[2:2 + 2 * couples:2]
    slack = jnp.minimum(giver - 1, reach - sink)
    moved = jax.random.randint(jax.random.fold_in(key, 1), (couples,), 0, 1 << 20) % (slack + 1)
    sizes = sizes.at[1:1 + 2 * couples:2].set(giver - moved).at[2:2 + 2 * couples:2].set(sink + moved)
    return sizes[jax.random.permutation(jax.random.fold_in(key, 2), amount)]


def gaussian(rng, shape, scale, limit, cuts=(), kind=jnp.bfloat16):
    drawn = jax.random.normal(rng, shape, jnp.float32) * scale
    if len(cuts) > 0:
        drawn = level_of(rng, shape, cuts, -0.22, 0.18) * drawn
    return jnp.clip(drawn, min=-limit, max=limit).astype(kind)


def setup_inputs(seed: int = 0) -> dict:
    seeds = jax.random.split(jax.random.key(seed), 9)
    return {
        "queries": draw_queries(jax.random.fold_in(seeds[8], 71), 0),
        "passages": draw_passages(jax.random.fold_in(seeds[8], 71), 0),
        "candidates": draw_candidates(jax.random.fold_in(seeds[8], 71), 0),
        "counts": ragged(seeds[3], NQB, 2 * NQB, C_MAX, 2).astype(jnp.int32),
        "teacher": draw_teacher(jax.random.fold_in(seeds[8], 71), 0),
        "section_weights": gaussian(seeds[5], (N_SECTION, D, D), D ** -0.5, 0.09375, ((0, 8), (1, 64))),
        "section_inputs": gaussian(seeds[6], (N_SECTION, M, D), 0.25, 1.5, ((0, 8), (2, 64))),
        "pre_acts": gaussian(seeds[7], (N_SECTION, M, D), 1.5, 8.0, ((0, 8), (2, 64))),
    }


INVERSE_TEMP = 20.0


def soft_weights(logits, valid):
    masked = jnp.where(valid, logits, -1e30)
    highest = jnp.max(masked, axis=-1, keepdims=True)
    expons = jnp.where(valid, jnp.exp(masked - highest), 0.0)
    return expons / jnp.sum(expons, axis=-1, keepdims=True)


def reference(queries, passages, candidates, counts, teacher, section_weights, section_inputs, pre_acts):
    query_blocks = queries.reshape(NQB, BLOCK, D)
    teacher_blocks = teacher.reshape(NQB, BLOCK, C_MAX * BLOCK)
    slot_index = jnp.arange(C_MAX, dtype=jnp.int32)

    def one_block(dense, item):
        query_row_items, teacher_rows, chosen, how_many = item
        pulled_rows = jnp.take(passages, chosen, axis=1)
        columns = jnp.transpose(pulled_rows, (1, 0, 2)).reshape(C_MAX * BLOCK, D)
        logits = jnp.dot(query_row_items, columns.T, preferred_element_type=jnp.float32) * INVERSE_TEMP
        valid = jnp.repeat(slot_index < how_many, BLOCK)[None, :]
        weight_matrices = (soft_weights(logits, valid) - soft_weights(teacher_rows, valid)).astype(jnp.bfloat16)
        query_sums = jnp.dot(weight_matrices, columns, preferred_element_type=jnp.float32) * INVERSE_TEMP
        passage_sums = jnp.dot(weight_matrices.T, query_row_items, preferred_element_type=jnp.float32) * INVERSE_TEMP
        rounded = lax.optimization_barrier(passage_sums.astype(jnp.bfloat16))
        passage_sums = rounded.astype(jnp.float32)
        passage_sums = jnp.transpose(passage_sums.reshape(C_MAX, BLOCK, D), (1, 0, 2))
        dense = dense.at[:, chosen, :].add(passage_sums)
        return dense, (query_sums.astype(jnp.bfloat16), query_sums[:MB_DEV])

    start_dense = jnp.zeros((BLOCK, NPB, D), jnp.float32)
    dense, (query_grads, micro_rows) = lax.scan(
        one_block, start_dense, (query_blocks, teacher_blocks, candidates, counts))
    top = micro_rows.reshape(N_SECTION, N_DP, QB_DEV, MB_DEV, D)[N_SECTION - 1, :, 0].reshape(N_DP * MB_DEV, D)

    cotangent = top
    input_grads = []
    weight_list = []
    for section_pos in range(N_SECTION - 1, -1, -1):
        pre = pre_acts[section_pos].astype(jnp.float32)
        sigma = jax.nn.sigmoid(pre)
        inner = (cotangent * (sigma * (1.0 + pre * (1.0 - sigma)))).astype(jnp.bfloat16)
        weight_list.append(
            jnp.dot(section_inputs[section_pos].T, inner, preferred_element_type=jnp.float32).astype(jnp.bfloat16))
        cotangent = cotangent + jnp.dot(inner, section_weights[section_pos].T, preferred_element_type=jnp.float32)
        input_grads.append(cotangent)
    return (query_grads.reshape(NQ, D), dense.astype(jnp.bfloat16),
            jnp.stack(input_grads[::-1]), jnp.stack(weight_list[::-1]))
```

```python
import jax
import jax.numpy as jnp
from jax import lax
from jax.sharding import PartitionSpec as P

INVERSE_TEMP = 20.0


def passed_along(value, axis, steps):
    count = lax.axis_size(axis)
    initial, last = (max(0, -steps), min(count, count - steps))
    return lax.ppermute(value, axis, [(source, source + steps) for source in range(initial, last)])


def gathered_columns(value, axis):
    count = lax.axis_size(axis)
    copies = jnp.broadcast_to(value[None], (count,) + value.shape)
    pieces = lax.all_to_all(copies, axis, 0, 0, tiled=True)
    return jnp.transpose(pieces, (1, 0, 2)).reshape(value.shape[0], count * value.shape[1])


def soft_weights(logits, valid):
    masked = jnp.where(valid, logits, -1e30)
    highest = jnp.max(masked, axis=-1, keepdims=True)
    expons = jnp.where(valid, jnp.exp(masked - highest), 0.0)
    return expons / jnp.sum(expons, axis=-1, keepdims=True)


def body(queries, passages, candidates, counts, teacher, section_weights, section_inputs, pre_acts):
    dp_count = lax.axis_size("dp")
    dp_index = lax.axis_index("dp")
    stripe, block_total, width = passages.shape
    row_block_count = stripe * dp_count
    blocks_here = candidates.shape[0] // dp_count
    slot_count = candidates.shape[1]
    requests = blocks_here * slot_count
    all_slots = candidates.reshape(-1)
    outgoing = jnp.take(passages, all_slots, axis=1)
    pulled_rows = lax.all_to_all(outgoing, "dp", split_axis=1, concat_axis=0, tiled=True)
    pulled_rows = pulled_rows.reshape(row_block_count, blocks_here, slot_count, width)
    own_counts = lax.dynamic_slice_in_dim(counts, dp_index * blocks_here, blocks_here)
    slot_valid = jnp.arange(slot_count, dtype=jnp.int32)[None, :] < own_counts[:, None]
    column_valid = jnp.repeat(slot_valid, row_block_count, axis=1)[:, None, :]
    query_row_items = queries.reshape(blocks_here, row_block_count, width)
    logits = (
        jnp.einsum(
            "ixp,wifp->ixfw", query_row_items, pulled_rows, preferred_element_type=jnp.float32
        )
        * INVERSE_TEMP
    )
    logits = logits.reshape(blocks_here, row_block_count, slot_count * row_block_count)
    target_logits = soft_weights(
        teacher.reshape(blocks_here, row_block_count, slot_count * row_block_count), column_valid
    )
    weight_matrices = (soft_weights(logits, column_valid) - target_logits).astype(jnp.bfloat16)
    weight_matrices = weight_matrices.reshape(
        blocks_here, row_block_count, slot_count, row_block_count
    )
    query_sums = (
        jnp.einsum(
            "geal,lgay->gey", weight_matrices, pulled_rows, preferred_element_type=jnp.float32
        )
        * INVERSE_TEMP
    )
    passage_sums = (
        jnp.einsum(
            "fnyw,fnj->wfyj", weight_matrices, query_row_items, preferred_element_type=jnp.float32
        )
        * INVERSE_TEMP
    )
    block_terms = passage_sums.reshape(row_block_count, requests, width).astype(jnp.bfloat16)
    micro_count = section_inputs.shape[1] // dp_count
    col_width = width // dp_count
    micro_cols = jnp.transpose(
        query_sums[0, :micro_count].reshape(micro_count, dp_count, col_width), (1, 0, 2)
    )
    incoming_piece = lax.all_to_all(block_terms, "dp", split_axis=0, concat_axis=1, tiled=True)
    entry = lax.all_to_all(micro_cols, "dp", split_axis=0, concat_axis=1, tiled=True)
    onehot = (all_slots[:, None] == jnp.arange(block_total, dtype=jnp.int32)[None, :]).astype(
        jnp.float32
    )
    dense = jnp.einsum(
        "sjd,jn->snd",
        incoming_piece.astype(jnp.float32),
        onehot,
        precision=lax.Precision.HIGHEST,
        preferred_element_type=jnp.float32,
    )
    passage_out = lax.psum(dense, "section").astype(jnp.bfloat16)
    weight_rows = section_weights[0]
    input_cols = section_inputs[0]
    pre = pre_acts[0].astype(jnp.float32)
    sigma = jax.nn.sigmoid(pre)
    slope = sigma * (1.0 + pre * (1.0 - sigma))
    carry = entry.reshape(dp_count * micro_count, col_width)
    section_count = lax.axis_size("section")
    section_index = lax.axis_index("section")
    grad_cols = jnp.zeros_like(carry)
    grad_weight = jnp.zeros((col_width, width), jnp.float32)
    for section_turn in range(section_count):
        active_flag = section_count - 1 - section_turn
        inner = (carry * slope).astype(jnp.bfloat16)
        piece = gathered_columns(inner, "dp")
        back_sum = jnp.einsum("mj,ij->mi", piece, weight_rows, preferred_element_type=jnp.float32)
        weight_part = jnp.einsum("mi,mj->ij", input_cols, piece, preferred_element_type=jnp.float32)
        back_sum, layer_weight = (back_sum, weight_part)
        updated = carry + back_sum
        is_active = section_index == active_flag
        grad_cols = jnp.where(is_active, updated, grad_cols)
        grad_weight = jnp.where(is_active, layer_weight, grad_weight)
        if section_turn + 1 < section_count:
            carry = passed_along(updated, "section", -1)
    return (
        query_sums.reshape(blocks_here * row_block_count, width).astype(jnp.bfloat16),
        passage_out,
        grad_cols[None],
        grad_weight[None].astype(jnp.bfloat16),
    )


def solution(mesh):
    placed = (
        P(("section", "dp"), None),
        P("dp", None, None),
        P("section", None),
        P("section"),
        P(("section", "dp"), None),
        P("section", "dp", None),
        P("section", None, "dp"),
        P("section", None, "dp"),
    )
    return jax.shard_map(
        body,
        mesh=mesh,
        in_specs=placed,
        out_specs=(
            P(("section", "dp"), None),
            P("dp", None, None),
            P("section", None, "dp"),
            P("section", "dp", None),
        ),
        check_vma=False,
    )
```

```python
import jax
import jax.numpy as jnp
from jax import lax
from jax.sharding import PartitionSpec as P

INVERSE_TEMP = 20.0


def passed_along(value, axis, steps):
    count = lax.axis_size(axis)
    initial, last = (max(0, -steps), min(count, count - steps))
    return lax.ppermute(value, axis, [(source, source + steps) for source in range(initial, last)])


def gathered_columns(value, axis):
    count = lax.axis_size(axis)
    copies = jnp.broadcast_to(value[None], (count,) + value.shape)
    pieces = lax.all_to_all(copies, axis, 0, 0, tiled=True)
    return jnp.transpose(pieces, (1, 0, 2)).reshape(value.shape[0], count * value.shape[1])


def soft_weights(logits, valid):
    masked = jnp.where(valid, logits, -1e30)
    highest = jnp.max(masked, axis=-1, keepdims=True)
    expons = jnp.where(valid, jnp.exp(masked - highest), 0.0)
    return expons / jnp.sum(expons, axis=-1, keepdims=True)


def body(queries, passages, candidates, counts, teacher, section_weights, section_inputs, pre_acts):
    dp_count = lax.axis_size("dp")
    dp_index = lax.axis_index("dp")
    stripe, block_total, width = passages.shape
    row_block_count = stripe * dp_count
    blocks_here = candidates.shape[0] // dp_count
    slot_count = candidates.shape[1]
    requests = blocks_here * slot_count
    all_slots = candidates.reshape(-1)
    chooser = (all_slots[:, None] == jnp.arange(block_total, dtype=jnp.int32)[None, :]).astype(
        passages.dtype
    )
    outgoing = jnp.einsum(
        "rpj,sp->rsj", passages, chooser, preferred_element_type=jnp.float32
    ).astype(passages.dtype)
    pulled_rows = lax.all_to_all(outgoing, "dp", split_axis=1, concat_axis=0, tiled=True)
    pulled_rows = pulled_rows.reshape(row_block_count, blocks_here, slot_count, width)
    own_counts = lax.dynamic_slice_in_dim(counts, dp_index * blocks_here, blocks_here)
    slot_valid = jnp.arange(slot_count, dtype=jnp.int32)[None, :] < own_counts[:, None]
    column_valid = jnp.repeat(slot_valid, row_block_count, axis=1)[:, None, :]
    query_row_items = queries.reshape(blocks_here, row_block_count, width)
    logits = (
        jnp.einsum(
            "ixp,wifp->ixfw", query_row_items, pulled_rows, preferred_element_type=jnp.float32
        )
        * INVERSE_TEMP
    )
    logits = logits.reshape(blocks_here, row_block_count, slot_count * row_block_count)
    target_logits = soft_weights(
        teacher.reshape(blocks_here, row_block_count, slot_count * row_block_count), column_valid
    )
    weight_matrices = (soft_weights(logits, column_valid) - target_logits).astype(jnp.bfloat16)
    weight_matrices = weight_matrices.reshape(
        blocks_here, row_block_count, slot_count, row_block_count
    )
    query_sums = (
        jnp.einsum(
            "geal,lgay->gey", weight_matrices, pulled_rows, preferred_element_type=jnp.float32
        )
        * INVERSE_TEMP
    )
    passage_sums = (
        jnp.einsum(
            "fnyw,fnj->wfyj", weight_matrices, query_row_items, preferred_element_type=jnp.float32
        )
        * INVERSE_TEMP
    )
    block_terms = passage_sums.reshape(row_block_count, requests, width).astype(jnp.bfloat16)
    micro_count = section_inputs.shape[1] // dp_count
    col_width = width // dp_count
    micro_cols = jnp.transpose(
        query_sums[0, :micro_count].reshape(micro_count, dp_count, col_width), (1, 0, 2)
    )
    section_count = lax.axis_size("section")
    chunk = width // section_count
    term_pieces = passage_sums.reshape(dp_count, stripe, requests, section_count, chunk)
    term_pieces = jnp.transpose(term_pieces, (3, 0, 1, 2, 4)).astype(jnp.bfloat16)
    term_pieces = term_pieces.reshape(section_count * dp_count, stripe, requests, chunk)
    incoming_terms = lax.all_to_all(
        term_pieces, ("section", "dp"), split_axis=0, concat_axis=0, tiled=True
    )
    every_slot = lax.all_gather(candidates, "section", axis=0, tiled=True)
    onehot = (every_slot[:, :, None] == jnp.arange(block_total, dtype=jnp.int32)).astype(
        jnp.bfloat16
    )
    dense = jnp.einsum(
        "qsfc,qfn->snc",
        incoming_terms.reshape(-1, stripe, slot_count, chunk),
        onehot.reshape(-1, slot_count, block_total),
        preferred_element_type=jnp.float32,
    )
    dense = dense.reshape(stripe, block_total, chunk).astype(jnp.bfloat16)
    passage_out = gathered_columns(dense.reshape(stripe * block_total, chunk), "section")
    passage_out = passage_out.reshape(stripe, block_total, width)
    entry = lax.all_to_all(micro_cols, "dp", split_axis=0, concat_axis=1, tiled=True)
    weight_rows = section_weights[0]
    input_cols = section_inputs[0]
    pre = pre_acts[0].astype(jnp.float32)
    sigma = jax.nn.sigmoid(pre)
    slope = sigma * (1.0 + pre * (1.0 - sigma))
    carry = entry.reshape(dp_count * micro_count, col_width)
    section_count = lax.axis_size("section")
    section_index = lax.axis_index("section")
    grad_cols = jnp.zeros_like(carry)
    grad_weight = jnp.zeros((col_width, width), jnp.float32)
    for section_turn in range(section_count):
        active_flag = section_count - 1 - section_turn
        inner = (carry * slope).astype(jnp.bfloat16)
        piece = gathered_columns(inner, "dp")
        back_sum = jnp.einsum("mj,ij->mi", piece, weight_rows, preferred_element_type=jnp.float32)
        weight_part = jnp.einsum("mi,mj->ij", input_cols, piece, preferred_element_type=jnp.float32)
        back_sum, layer_weight = (back_sum, weight_part)
        updated = carry + back_sum
        is_active = section_index == active_flag
        grad_cols = jnp.where(is_active, updated, grad_cols)
        grad_weight = jnp.where(is_active, layer_weight, grad_weight)
        if section_turn + 1 < section_count:
            carry = passed_along(updated, "section", -1)
    return (
        query_sums.reshape(blocks_here * row_block_count, width).astype(jnp.bfloat16),
        passage_out,
        grad_cols[None],
        grad_weight[None].astype(jnp.bfloat16),
    )


def solution(mesh):
    placed = (
        P(("section", "dp"), None),
        P("dp", None, None),
        P("section", None),
        P("section"),
        P(("section", "dp"), None),
        P("section", "dp", None),
        P("section", None, "dp"),
        P("section", None, "dp"),
    )
    return jax.shard_map(
        body,
        mesh=mesh,
        in_specs=placed,
        out_specs=(
            P(("section", "dp"), None),
            P("dp", None, None),
            P("section", None, "dp"),
            P("section", "dp", None),
        ),
        check_vma=False,
    )
```

```python
import jax
import jax.numpy as jnp
from jax import lax
from jax.sharding import PartitionSpec as P

INVERSE_TEMP = 20.0


def passed_along(value, axis, steps):
    count = lax.axis_size(axis)
    initial, last = (max(0, -steps), min(count, count - steps))
    return lax.ppermute(value, axis, [(source, source + steps) for source in range(initial, last)])


def gathered_pieces(value, axis):
    count = lax.axis_size(axis)
    copies = jnp.broadcast_to(value[None], (count,) + value.shape)
    return lax.all_to_all(copies, axis, 0, 0, tiled=True)


def gathered_columns(value, axis):
    count = lax.axis_size(axis)
    copies = jnp.broadcast_to(value[None], (count,) + value.shape)
    pieces = lax.all_to_all(copies, axis, 0, 0, tiled=True)
    return jnp.transpose(pieces, (1, 0, 2)).reshape(value.shape[0], count * value.shape[1])


def soft_weights(logits, valid):
    masked = jnp.where(valid, logits, -1e30)
    highest = jnp.max(masked, axis=-1, keepdims=True)
    expons = jnp.where(valid, jnp.exp(masked - highest), 0.0)
    return expons / jnp.sum(expons, axis=-1, keepdims=True)


def body(queries, passages, candidates, counts, teacher, section_weights, section_inputs, pre_acts):
    dp_count = lax.axis_size("dp")
    dp_index = lax.axis_index("dp")
    stripe, block_total, width = passages.shape
    row_block_count = stripe * dp_count
    blocks_here = candidates.shape[0] // dp_count
    slot_count = candidates.shape[1]
    requests = blocks_here * slot_count
    all_slots = candidates.reshape(-1)
    chooser = (all_slots[:, None] == jnp.arange(block_total, dtype=jnp.int32)[None, :]).astype(
        passages.dtype
    )
    outgoing = jnp.einsum(
        "rpj,sp->rsj", passages, chooser, preferred_element_type=jnp.float32
    ).astype(passages.dtype)
    pulled_rows = lax.all_to_all(outgoing, "dp", split_axis=1, concat_axis=0, tiled=True)
    pulled_rows = pulled_rows.reshape(row_block_count, blocks_here, slot_count, width)
    own_counts = lax.dynamic_slice_in_dim(counts, dp_index * blocks_here, blocks_here)
    slot_valid = jnp.arange(slot_count, dtype=jnp.int32)[None, :] < own_counts[:, None]
    column_valid = jnp.repeat(slot_valid, row_block_count, axis=1)[:, None, :]
    query_row_items = queries.reshape(blocks_here, row_block_count, width)
    logits = (
        jnp.einsum(
            "ixp,wifp->ixfw", query_row_items, pulled_rows, preferred_element_type=jnp.float32
        )
        * INVERSE_TEMP
    )
    logits = logits.reshape(blocks_here, row_block_count, slot_count * row_block_count)
    target_logits = soft_weights(
        teacher.reshape(blocks_here, row_block_count, slot_count * row_block_count), column_valid
    )
    weight_matrices = (soft_weights(logits, column_valid) - target_logits).astype(jnp.bfloat16)
    weight_matrices = weight_matrices.reshape(
        blocks_here, row_block_count, slot_count, row_block_count
    )
    query_sums = (
        jnp.einsum(
            "geal,lgay->gey", weight_matrices, pulled_rows, preferred_element_type=jnp.float32
        )
        * INVERSE_TEMP
    )
    passage_sums = (
        jnp.einsum(
            "fnyw,fnj->wfyj", weight_matrices, query_row_items, preferred_element_type=jnp.float32
        )
        * INVERSE_TEMP
    )
    block_terms = passage_sums.reshape(row_block_count, requests, width).astype(jnp.bfloat16)
    micro_count = section_inputs.shape[1] // dp_count
    col_width = width // dp_count
    micro_cols = jnp.transpose(
        query_sums[0, :micro_count].reshape(micro_count, dp_count, col_width), (1, 0, 2)
    )
    section_count = lax.axis_size("section")
    chunk = width // section_count
    term_pieces = passage_sums.reshape(dp_count, stripe, requests, section_count, chunk)
    term_pieces = jnp.transpose(term_pieces, (3, 0, 1, 2, 4)).astype(jnp.bfloat16)
    term_pieces = term_pieces.reshape(section_count * dp_count, stripe, requests, chunk)
    own_slots = lax.dynamic_slice_in_dim(all_slots, dp_index * requests, requests)
    slot_tags = jnp.broadcast_to(
        own_slots.astype(jnp.bfloat16)[None, None, :, None],
        (section_count * dp_count, stripe, requests, 1),
    )
    term_pieces = jnp.concatenate([term_pieces, slot_tags], axis=3)
    incoming_terms = lax.all_to_all(
        term_pieces, ("section", "dp"), split_axis=0, concat_axis=0, tiled=True
    )
    incoming_terms, carry_start = lax.optimization_barrier((incoming_terms, micro_cols))
    every_slot = incoming_terms[:, 0, :, chunk].astype(jnp.int32)
    onehot = (every_slot[:, :, None] == jnp.arange(block_total, dtype=jnp.int32)).astype(
        jnp.bfloat16
    )
    dense = jnp.einsum(
        "qsfc,qfn->snc",
        incoming_terms[:, :, :, :chunk],
        onehot,
        preferred_element_type=jnp.float32,
    )
    dense = dense.reshape(stripe, block_total, chunk).astype(jnp.bfloat16)
    passage_out = gathered_columns(dense.reshape(stripe * block_total, chunk), "section")
    passage_out = passage_out.reshape(stripe, block_total, width)
    entry = lax.all_to_all(carry_start, "dp", split_axis=0, concat_axis=1, tiled=True)
    weight_rows = section_weights[0]
    split_rows = weight_rows.reshape(col_width, dp_count, col_width)
    input_cols = section_inputs[0]
    pre = pre_acts[0].astype(jnp.float32)
    sigma = jax.nn.sigmoid(pre)
    slope = sigma * (1.0 + pre * (1.0 - sigma))
    carry = entry.reshape(dp_count * micro_count, col_width)
    section_count = lax.axis_size("section")
    section_index = lax.axis_index("section")
    grad_cols = jnp.zeros_like(carry)
    grad_weight = jnp.zeros((col_width, width), jnp.float32)
    for section_turn in range(section_count):
        active_flag = section_count - 1 - section_turn
        inner = (carry * slope).astype(jnp.bfloat16)
        piece = gathered_pieces(inner, "dp")
        back_sum = jnp.einsum(
            "dmj,idj->mi", piece, split_rows, preferred_element_type=jnp.float32
        )
        weight_part = jnp.einsum(
            "mi,dmj->idj", input_cols, piece, preferred_element_type=jnp.float32
        ).reshape(col_width, width)
        back_sum, layer_weight = (back_sum, weight_part)
        updated = carry + back_sum
        is_active = section_index == active_flag
        grad_cols = jnp.where(is_active, updated, grad_cols)
        grad_weight = jnp.where(is_active, layer_weight, grad_weight)
        if section_turn + 1 < section_count:
            carry = passed_along(updated, "section", -1)
    return (
        query_sums.reshape(blocks_here * row_block_count, width).astype(jnp.bfloat16),
        passage_out,
        grad_cols[None],
        grad_weight[None].astype(jnp.bfloat16),
    )


def solution(mesh):
    placed = (
        P(("section", "dp"), None),
        P("dp", None, None),
        P("section", None),
        P("section"),
        P(("section", "dp"), None),
        P("section", "dp", None),
        P("section", None, "dp"),
        P("section", None, "dp"),
    )
    return jax.shard_map(
        body,
        mesh=mesh,
        in_specs=placed,
        out_specs=(
            P(("section", "dp"), None),
            P("dp", None, None),
            P("section", None, "dp"),
            P("section", "dp", None),
        ),
        check_vma=False,
    )
```

```python
import jax
import jax.numpy as jnp
from jax import lax
from jax.sharding import PartitionSpec as P

INVERSE_TEMP = 20.0


def passed_along(value, axis, steps):
    count = lax.axis_size(axis)
    initial, last = (max(0, -steps), min(count, count - steps))
    return lax.ppermute(value, axis, [(source, source + steps) for source in range(initial, last)])


def gathered_pieces(value, axis):
    count = lax.axis_size(axis)
    copies = jnp.broadcast_to(value[None], (count,) + value.shape)
    return lax.all_to_all(copies, axis, 0, 0, tiled=True)


def gathered_columns(value, axis):
    count = lax.axis_size(axis)
    copies = jnp.broadcast_to(value[None], (count,) + value.shape)
    pieces = lax.all_to_all(copies, axis, 0, 0, tiled=True)
    return jnp.transpose(pieces, (1, 0, 2)).reshape(value.shape[0], count * value.shape[1])


def soft_weights(logits, valid):
    masked = jnp.where(valid, logits, -1e30)
    highest = jnp.max(masked, axis=-1, keepdims=True)
    expons = jnp.where(valid, jnp.exp(masked - highest), 0.0)
    return expons / jnp.sum(expons, axis=-1, keepdims=True)


def body(queries, passages, candidates, counts, teacher, section_weights, section_inputs, pre_acts):
    dp_count = lax.axis_size("dp")
    dp_index = lax.axis_index("dp")
    stripe, block_total, width = passages.shape
    row_block_count = stripe * dp_count
    blocks_here = candidates.shape[0] // dp_count
    slot_count = candidates.shape[1]
    requests = blocks_here * slot_count
    all_slots = candidates.reshape(-1)
    chooser = (all_slots[:, None] == jnp.arange(block_total, dtype=jnp.int32)[None, :]).astype(
        passages.dtype
    )
    outgoing = jnp.einsum(
        "rpj,sp->rsj", passages, chooser, preferred_element_type=jnp.float32
    ).astype(passages.dtype)
    pulled_rows = lax.all_to_all(outgoing, "dp", split_axis=1, concat_axis=0, tiled=True)
    pulled_rows = pulled_rows.reshape(row_block_count, blocks_here, slot_count, width)
    own_counts = lax.dynamic_slice_in_dim(counts, dp_index * blocks_here, blocks_here)
    slot_valid = jnp.arange(slot_count, dtype=jnp.int32)[None, :] < own_counts[:, None]
    column_valid = jnp.repeat(slot_valid, row_block_count, axis=1)[:, None, :]
    query_row_items = queries.reshape(blocks_here, row_block_count, width)
    logits = (
        jnp.einsum(
            "ixp,wifp->ixfw", query_row_items, pulled_rows, preferred_element_type=jnp.float32
        )
        * INVERSE_TEMP
    )
    logits = logits.reshape(blocks_here, row_block_count, slot_count * row_block_count)
    target_logits = soft_weights(
        teacher.reshape(blocks_here, row_block_count, slot_count * row_block_count), column_valid
    )
    weight_matrices = (soft_weights(logits, column_valid) - target_logits).astype(jnp.bfloat16)
    weight_matrices = weight_matrices.reshape(
        blocks_here, row_block_count, slot_count, row_block_count
    )
    query_sums = (
        jnp.einsum(
            "geal,lgay->gey", weight_matrices, pulled_rows, preferred_element_type=jnp.float32
        )
        * INVERSE_TEMP
    )
    passage_sums = (
        jnp.einsum(
            "fnyw,fnj->wfyj", weight_matrices, query_row_items, preferred_element_type=jnp.float32
        )
        * INVERSE_TEMP
    )
    block_terms = passage_sums.reshape(row_block_count, requests, width).astype(jnp.bfloat16)
    micro_count = section_inputs.shape[1] // dp_count
    col_width = width // dp_count
    micro_cols = jnp.transpose(
        query_sums[0, :micro_count].reshape(micro_count, dp_count, col_width), (1, 0, 2)
    )
    section_count = lax.axis_size("section")
    chunk = width // section_count
    term_pieces = passage_sums.reshape(dp_count, stripe, requests, section_count, chunk)
    term_pieces = jnp.transpose(term_pieces, (3, 0, 1, 2, 4)).astype(jnp.bfloat16)
    term_pieces = term_pieces.reshape(section_count * dp_count, stripe, requests, chunk)
    own_slots = lax.dynamic_slice_in_dim(all_slots, dp_index * requests, requests)
    slot_tags = jnp.broadcast_to(
        own_slots.astype(jnp.bfloat16)[None, None, :, None],
        (section_count * dp_count, stripe, requests, 1),
    )
    term_pieces = jnp.concatenate([term_pieces, slot_tags], axis=3)
    incoming_terms = lax.all_to_all(
        term_pieces, ("section", "dp"), split_axis=0, concat_axis=0, tiled=True
    )
    incoming_terms, carry_start = lax.optimization_barrier((incoming_terms, micro_cols))
    every_slot = incoming_terms[:, 0, :, chunk].astype(jnp.int32)
    onehot = (every_slot[:, :, None] == jnp.arange(block_total, dtype=jnp.int32)).astype(
        jnp.bfloat16
    )
    dense = jnp.einsum(
        "qsfc,qfn->snc",
        incoming_terms[:, :, :, :chunk],
        onehot,
        preferred_element_type=jnp.float32,
    )
    dense = dense.reshape(stripe, block_total, chunk).astype(jnp.bfloat16)
    passage_out = gathered_columns(dense.reshape(stripe * block_total, chunk), "section")
    passage_out = passage_out.reshape(stripe, block_total, width)
    entry = lax.all_to_all(carry_start, "dp", split_axis=0, concat_axis=1, tiled=True)
    section_count = lax.axis_size("section")
    section_index = lax.axis_index("section")
    last = section_count - 1
    own_rows = section_weights[0]
    own_cols = jnp.stack([pre_acts[0], section_inputs[0]])
    rows_of = {last: own_rows}
    cols_of = {last: own_cols}
    for source in range(last):
        rows_of[source] = lax.ppermute(own_rows, "section", [(source, last)])
        cols_of[source] = lax.ppermute(own_cols, "section", [(source, last)])
    carry = entry.reshape(dp_count * micro_count, col_width)
    grads_of = {}
    weights_of = {}
    for source in range(last, -1, -1):
        pre = cols_of[source][0].astype(jnp.float32)
        sigma = jax.nn.sigmoid(pre)
        slope = sigma * (1.0 + pre * (1.0 - sigma))
        inner = (carry * slope).astype(jnp.bfloat16)
        piece = gathered_pieces(inner, "dp")
        split_rows = rows_of[source].reshape(col_width, dp_count, col_width)
        back_sum = jnp.einsum(
            "dmj,idj->mi", piece, split_rows, preferred_element_type=jnp.float32
        )
        weights_of[source] = (
            jnp.einsum(
                "mi,dmj->idj", cols_of[source][1], piece, preferred_element_type=jnp.float32
            )
            .reshape(col_width, width)
            .astype(jnp.bfloat16)
        )
        carry = carry + back_sum
        grads_of[source] = carry
    grad_cols = grads_of[last]
    grad_weight = weights_of[last]
    for source in range(last):
        sent_grads = lax.ppermute(grads_of[source], "section", [(last, source)])
        sent_weights = lax.ppermute(weights_of[source], "section", [(last, source)])
        grad_cols = jnp.where(section_index == source, sent_grads, grad_cols)
        grad_weight = jnp.where(section_index == source, sent_weights, grad_weight)
    return (
        query_sums.reshape(blocks_here * row_block_count, width).astype(jnp.bfloat16),
        passage_out,
        grad_cols[None],
        grad_weight[None],
    )


def solution(mesh):
    placed = (
        P(("section", "dp"), None),
        P("dp", None, None),
        P("section", None),
        P("section"),
        P(("section", "dp"), None),
        P("section", "dp", None),
        P("section", None, "dp"),
        P("section", None, "dp"),
    )
    return jax.shard_map(
        body,
        mesh=mesh,
        in_specs=placed,
        out_specs=(
            P(("section", "dp"), None),
            P("dp", None, None),
            P("section", None, "dp"),
            P("section", "dp", None),
        ),
        check_vma=False,
    )
```

```python
import jax
import jax.numpy as jnp
from jax import lax
from jax.sharding import PartitionSpec as P

INVERSE_TEMP = 20.0


def passed_along(value, axis, steps):
    count = lax.axis_size(axis)
    initial, last = (max(0, -steps), min(count, count - steps))
    return lax.ppermute(value, axis, [(source, source + steps) for source in range(initial, last)])


def gathered_pieces(value, axis):
    count = lax.axis_size(axis)
    copies = jnp.broadcast_to(value[None], (count,) + value.shape)
    return lax.all_to_all(copies, axis, 0, 0, tiled=True)


def gathered_columns(value, axis):
    count = lax.axis_size(axis)
    copies = jnp.broadcast_to(value[None], (count,) + value.shape)
    pieces = lax.all_to_all(copies, axis, 0, 0, tiled=True)
    return jnp.transpose(pieces, (1, 0, 2)).reshape(value.shape[0], count * value.shape[1])


def soft_weights(logits, valid):
    masked = jnp.where(valid, logits, -1e30)
    highest = jnp.max(masked, axis=-1, keepdims=True)
    expons = jnp.where(valid, jnp.exp(masked - highest), 0.0)
    return expons / jnp.sum(expons, axis=-1, keepdims=True)


def body(queries, passages, candidates, counts, teacher, section_weights, section_inputs, pre_acts):
    dp_count = lax.axis_size("dp")
    dp_index = lax.axis_index("dp")
    stripe, block_total, width = passages.shape
    row_block_count = stripe * dp_count
    blocks_here = candidates.shape[0] // dp_count
    slot_count = candidates.shape[1]
    requests = blocks_here * slot_count
    all_slots = candidates.reshape(-1)
    chooser = (all_slots[:, None] == jnp.arange(block_total, dtype=jnp.int32)[None, :]).astype(
        passages.dtype
    )
    outgoing = jnp.einsum(
        "rpj,sp->rsj", passages, chooser, preferred_element_type=jnp.float32
    ).astype(passages.dtype)
    pulled_rows = lax.all_to_all(outgoing, "dp", split_axis=1, concat_axis=0, tiled=True)
    pulled_rows = pulled_rows.reshape(row_block_count, blocks_here, slot_count, width)
    own_counts = lax.dynamic_slice_in_dim(counts, dp_index * blocks_here, blocks_here)
    slot_valid = jnp.arange(slot_count, dtype=jnp.int32)[None, :] < own_counts[:, None]
    column_valid = jnp.repeat(slot_valid, row_block_count, axis=1)[:, None, :]
    query_row_items = queries.reshape(blocks_here, row_block_count, width)
    logits = (
        jnp.einsum(
            "ixp,wifp->ixfw", query_row_items, pulled_rows, preferred_element_type=jnp.float32
        )
        * INVERSE_TEMP
    )
    logits = logits.reshape(blocks_here, row_block_count, slot_count * row_block_count)
    target_logits = soft_weights(
        teacher.reshape(blocks_here, row_block_count, slot_count * row_block_count), column_valid
    )
    weight_matrices = (soft_weights(logits, column_valid) - target_logits).astype(jnp.bfloat16)
    weight_matrices = weight_matrices.reshape(
        blocks_here, row_block_count, slot_count, row_block_count
    )
    query_sums = (
        jnp.einsum(
            "geal,lgay->gey", weight_matrices, pulled_rows, preferred_element_type=jnp.float32
        )
        * INVERSE_TEMP
    )
    passage_sums = (
        jnp.einsum(
            "fnyw,fnj->wfyj", weight_matrices, query_row_items, preferred_element_type=jnp.float32
        )
        * INVERSE_TEMP
    )
    block_terms = passage_sums.reshape(row_block_count, requests, width).astype(jnp.bfloat16)
    micro_count = section_inputs.shape[1] // dp_count
    col_width = width // dp_count
    micro_cols = jnp.transpose(
        query_sums[0, :micro_count].reshape(micro_count, dp_count, col_width), (1, 0, 2)
    )
    section_count = lax.axis_size("section")
    chunk = width // section_count
    term_pieces = passage_sums.reshape(dp_count, stripe, requests, section_count, chunk)
    term_pieces = jnp.transpose(term_pieces, (3, 0, 1, 2, 4)).astype(jnp.bfloat16)
    term_pieces = term_pieces.reshape(section_count * dp_count, stripe, requests, chunk)
    own_slots = lax.dynamic_slice_in_dim(all_slots, dp_index * requests, requests)
    slot_tags = jnp.broadcast_to(
        own_slots.astype(jnp.bfloat16)[None, None, :, None],
        (section_count * dp_count, stripe, requests, 1),
    )
    term_pieces = jnp.concatenate([term_pieces, slot_tags], axis=3)
    incoming_terms = lax.all_to_all(
        term_pieces, ("section", "dp"), split_axis=0, concat_axis=0, tiled=True
    )
    last_section = section_count - 1
    packed = jnp.concatenate(
        [
            section_weights[0].reshape(col_width, dp_count, col_width),
            pre_acts[0][None],
        ]
    )
    moved = tuple(
        lax.ppermute(packed, "section", [(source, last_section)]) for source in range(last_section)
    )
    incoming_terms, carry_start, moved = lax.optimization_barrier(
        (incoming_terms, micro_cols, moved)
    )
    packed_of = dict(enumerate(moved))
    packed_of[last_section] = packed
    every_slot = incoming_terms[:, 0, :, chunk].astype(jnp.int32)
    onehot = (every_slot[:, :, None] == jnp.arange(block_total, dtype=jnp.int32)).astype(
        jnp.bfloat16
    )
    dense = jnp.einsum(
        "qsfc,qfn->snc",
        incoming_terms[:, :, :, :chunk],
        onehot,
        preferred_element_type=jnp.float32,
    )
    dense = dense.reshape(stripe, block_total, chunk).astype(jnp.bfloat16)
    passage_out = gathered_columns(dense.reshape(stripe * block_total, chunk), "section")
    passage_out = passage_out.reshape(stripe, block_total, width)
    entry = lax.all_to_all(carry_start, "dp", split_axis=0, concat_axis=1, tiled=True)
    section_index = lax.axis_index("section")
    last = section_count - 1
    carry = entry.reshape(dp_count * micro_count, col_width)
    sent_of = {}
    for source in range(last, -1, -1):
        rows = packed_of[source][:col_width]
        pre = packed_of[source][col_width].astype(jnp.float32)
        sigma = jax.nn.sigmoid(pre)
        slope = sigma * (1.0 + pre * (1.0 - sigma))
        inner = (carry * slope).astype(jnp.bfloat16)
        piece = gathered_pieces(inner, "dp")
        back_sum = jnp.einsum("dmj,idj->mi", piece, rows, preferred_element_type=jnp.float32)
        carry = carry + back_sum
        if source == last:
            grad_cols, home_inner = carry, inner
        else:
            both = jnp.stack([carry, inner.astype(jnp.float32)])
            sent_of[source] = lax.ppermute(both, "section", [(last, source)])
    for source in range(last):
        here = section_index == source
        grad_cols = jnp.where(here, sent_of[source][0], grad_cols)
        home_inner = jnp.where(here, sent_of[source][1].astype(jnp.bfloat16), home_inner)
    home_piece = gathered_pieces(home_inner, "dp")
    grad_weight = (
        jnp.einsum("mi,dmj->idj", section_inputs[0], home_piece, preferred_element_type=jnp.float32)
        .reshape(col_width, width)
        .astype(jnp.bfloat16)
    )
    return (
        query_sums.reshape(blocks_here * row_block_count, width).astype(jnp.bfloat16),
        passage_out,
        grad_cols[None],
        grad_weight[None],
    )


def solution(mesh):
    placed = (
        P(("section", "dp"), None),
        P("dp", None, None),
        P("section", None),
        P("section"),
        P(("section", "dp"), None),
        P("section", "dp", None),
        P("section", None, "dp"),
        P("section", None, "dp"),
    )
    return jax.shard_map(
        body,
        mesh=mesh,
        in_specs=placed,
        out_specs=(
            P(("section", "dp"), None),
            P("dp", None, None),
            P("section", None, "dp"),
            P("section", "dp", None),
        ),
        check_vma=False,
    )
```

```python
import jax
import jax.numpy as jnp
from jax import lax
from jax.sharding import PartitionSpec as P

INVERSE_TEMP = 20.0


def passed_along(value, axis, steps):
    count = lax.axis_size(axis)
    initial, last = (max(0, -steps), min(count, count - steps))
    return lax.ppermute(value, axis, [(source, source + steps) for source in range(initial, last)])


def gathered_pieces(value, axis):
    count = lax.axis_size(axis)
    copies = jnp.broadcast_to(value[None], (count,) + value.shape)
    return lax.all_to_all(copies, axis, 0, 0, tiled=True)


def gathered_columns(value, axis):
    count = lax.axis_size(axis)
    copies = jnp.broadcast_to(value[None], (count,) + value.shape)
    pieces = lax.all_to_all(copies, axis, 0, 0, tiled=True)
    return jnp.transpose(pieces, (1, 0, 2)).reshape(value.shape[0], count * value.shape[1])


def soft_weights(logits, valid):
    masked = jnp.where(valid, logits, -1e30)
    highest = jnp.max(masked, axis=-1, keepdims=True)
    expons = jnp.where(valid, jnp.exp(masked - highest), 0.0)
    return expons / jnp.sum(expons, axis=-1, keepdims=True)


def body(queries, passages, candidates, counts, teacher, section_weights, section_inputs, pre_acts):
    dp_count = lax.axis_size("dp")
    dp_index = lax.axis_index("dp")
    stripe, block_total, width = passages.shape
    row_block_count = stripe * dp_count
    blocks_here = candidates.shape[0] // dp_count
    slot_count = candidates.shape[1]
    requests = blocks_here * slot_count
    all_slots = candidates.reshape(-1)
    chooser = (all_slots[:, None] == jnp.arange(block_total, dtype=jnp.int32)[None, :]).astype(
        passages.dtype
    )
    outgoing = jnp.einsum(
        "rpj,sp->rsj", passages, chooser, preferred_element_type=jnp.float32
    ).astype(passages.dtype)
    col_width = width // dp_count
    section_count = lax.axis_size("section")
    last_section = section_count - 1
    packed = jnp.concatenate(
        [
            section_weights[0].reshape(col_width, dp_count, col_width),
            pre_acts[0][None],
        ]
    )
    moved = tuple(
        lax.ppermute(packed, "section", [(source, last_section)]) for source in range(last_section)
    )
    pulled_rows = lax.all_to_all(outgoing, "dp", split_axis=1, concat_axis=0, tiled=True)
    pulled_rows, moved = lax.optimization_barrier((pulled_rows, moved))
    packed_of = dict(enumerate(moved))
    packed_of[last_section] = packed
    pulled_rows = pulled_rows.reshape(row_block_count, blocks_here, slot_count, width)
    own_counts = lax.dynamic_slice_in_dim(counts, dp_index * blocks_here, blocks_here)
    slot_valid = jnp.arange(slot_count, dtype=jnp.int32)[None, :] < own_counts[:, None]
    column_valid = jnp.repeat(slot_valid, row_block_count, axis=1)[:, None, :]
    query_row_items = queries.reshape(blocks_here, row_block_count, width)
    logits = (
        jnp.einsum(
            "ixp,wifp->ixfw", query_row_items, pulled_rows, preferred_element_type=jnp.float32
        )
        * INVERSE_TEMP
    )
    logits = logits.reshape(blocks_here, row_block_count, slot_count * row_block_count)
    target_logits = soft_weights(
        teacher.reshape(blocks_here, row_block_count, slot_count * row_block_count), column_valid
    )
    weight_matrices = (soft_weights(logits, column_valid) - target_logits).astype(jnp.bfloat16)
    weight_matrices = weight_matrices.reshape(
        blocks_here, row_block_count, slot_count, row_block_count
    )
    query_sums = (
        jnp.einsum(
            "geal,lgay->gey", weight_matrices, pulled_rows, preferred_element_type=jnp.float32
        )
        * INVERSE_TEMP
    )
    passage_sums = (
        jnp.einsum(
            "fnyw,fnj->wfyj", weight_matrices, query_row_items, preferred_element_type=jnp.float32
        )
        * INVERSE_TEMP
    )
    block_terms = passage_sums.reshape(row_block_count, requests, width).astype(jnp.bfloat16)
    micro_count = section_inputs.shape[1] // dp_count
    micro_cols = jnp.transpose(
        query_sums[0, :micro_count].reshape(micro_count, dp_count, col_width), (1, 0, 2)
    )
    section_count = lax.axis_size("section")
    chunk = width // section_count
    term_pieces = passage_sums.reshape(dp_count, stripe, requests, section_count, chunk)
    term_pieces = jnp.transpose(term_pieces, (3, 0, 1, 2, 4)).astype(jnp.bfloat16)
    term_pieces = term_pieces.reshape(section_count * dp_count, stripe, requests, chunk)
    own_slots = lax.dynamic_slice_in_dim(all_slots, dp_index * requests, requests)
    slot_tags = jnp.broadcast_to(
        own_slots.astype(jnp.bfloat16)[None, None, :, None],
        (section_count * dp_count, stripe, requests, 1),
    )
    term_pieces = jnp.concatenate([term_pieces, slot_tags], axis=3)
    entry = lax.all_to_all(micro_cols, "dp", split_axis=0, concat_axis=1, tiled=True)
    section_index = lax.axis_index("section")
    last = section_count - 1
    carry = entry.reshape(dp_count * micro_count, col_width)
    sent_of = {}
    for source in range(last, -1, -1):
        rows = packed_of[source][:col_width]
        pre = packed_of[source][col_width].astype(jnp.float32)
        sigma = jax.nn.sigmoid(pre)
        slope = sigma * (1.0 + pre * (1.0 - sigma))
        inner = (carry * slope).astype(jnp.bfloat16)
        piece = gathered_pieces(inner, "dp")
        back_sum = jnp.einsum("dmj,idj->mi", piece, rows, preferred_element_type=jnp.float32)
        carry = carry + back_sum
        if source == last:
            grad_cols, home_inner = carry, inner
        else:
            both = jnp.stack([carry, inner.astype(jnp.float32)])
            sent_of[source] = lax.ppermute(both, "section", [(last, source)])
    for source in range(last):
        here = section_index == source
        grad_cols = jnp.where(here, sent_of[source][0], grad_cols)
        home_inner = jnp.where(here, sent_of[source][1].astype(jnp.bfloat16), home_inner)
    term_pieces, carry = lax.optimization_barrier((term_pieces, carry))
    incoming_terms = lax.all_to_all(
        term_pieces, ("section", "dp"), split_axis=0, concat_axis=0, tiled=True
    )
    every_slot = incoming_terms[:, 0, :, chunk].astype(jnp.int32)
    onehot = (every_slot[:, :, None] == jnp.arange(block_total, dtype=jnp.int32)).astype(
        jnp.bfloat16
    )
    dense = jnp.einsum(
        "qsfc,qfn->snc",
        incoming_terms[:, :, :, :chunk],
        onehot,
        preferred_element_type=jnp.float32,
    )
    dense = dense.reshape(stripe, block_total, chunk).astype(jnp.bfloat16)
    passage_out = gathered_columns(dense.reshape(stripe * block_total, chunk), "section")
    passage_out = passage_out.reshape(stripe, block_total, width)
    home_piece = gathered_pieces(home_inner, "dp")
    grad_weight = (
        jnp.einsum("mi,dmj->idj", section_inputs[0], home_piece, preferred_element_type=jnp.float32)
        .reshape(col_width, width)
        .astype(jnp.bfloat16)
    )
    return (
        query_sums.reshape(blocks_here * row_block_count, width).astype(jnp.bfloat16),
        passage_out,
        grad_cols[None],
        grad_weight[None],
    )


def solution(mesh):
    placed = (
        P(("section", "dp"), None),
        P("dp", None, None),
        P("section", None),
        P("section"),
        P(("section", "dp"), None),
        P("section", "dp", None),
        P("section", None, "dp"),
        P("section", None, "dp"),
    )
    return jax.shard_map(
        body,
        mesh=mesh,
        in_specs=placed,
        out_specs=(
            P(("section", "dp"), None),
            P("dp", None, None),
            P("section", None, "dp"),
            P("section", "dp", None),
        ),
        check_vma=False,
    )
```

```python
import jax
import jax.numpy as jnp
from jax import lax
from jax.sharding import PartitionSpec as P

INVERSE_TEMP = 20.0


def passed_along(value, axis, steps):
    count = lax.axis_size(axis)
    initial, last = (max(0, -steps), min(count, count - steps))
    return lax.ppermute(value, axis, [(source, source + steps) for source in range(initial, last)])


def gathered_pieces(value, axis):
    count = lax.axis_size(axis)
    copies = jnp.broadcast_to(value[None], (count,) + value.shape)
    return lax.all_to_all(copies, axis, 0, 0, tiled=True)


def gathered_columns(value, axis):
    count = lax.axis_size(axis)
    copies = jnp.broadcast_to(value[None], (count,) + value.shape)
    pieces = lax.all_to_all(copies, axis, 0, 0, tiled=True)
    return jnp.transpose(pieces, (1, 0, 2)).reshape(value.shape[0], count * value.shape[1])


def soft_weights(logits, valid):
    masked = jnp.where(valid, logits, -1e30)
    highest = jnp.max(masked, axis=-1, keepdims=True)
    expons = jnp.where(valid, jnp.exp(masked - highest), 0.0)
    return expons / jnp.sum(expons, axis=-1, keepdims=True)


def body(queries, passages, candidates, counts, teacher, section_weights, section_inputs, pre_acts):
    dp_count = lax.axis_size("dp")
    dp_index = lax.axis_index("dp")
    stripe, block_total, width = passages.shape
    row_block_count = stripe * dp_count
    blocks_here = candidates.shape[0] // dp_count
    slot_count = candidates.shape[1]
    requests = blocks_here * slot_count
    all_slots = candidates.reshape(-1)
    chooser = (all_slots[:, None] == jnp.arange(block_total, dtype=jnp.int32)[None, :]).astype(
        passages.dtype
    )
    outgoing = jnp.einsum(
        "rpj,sp->rsj", passages, chooser, preferred_element_type=jnp.float32
    ).astype(passages.dtype)
    col_width = width // dp_count
    section_count = lax.axis_size("section")
    last_section = section_count - 1
    packed = jnp.concatenate(
        [
            section_weights[0].reshape(col_width, dp_count, col_width),
            pre_acts[0][None],
        ]
    )
    moved = tuple(
        lax.ppermute(packed, "section", [(source, last_section)]) for source in range(last_section)
    )
    pulled_rows = lax.all_to_all(outgoing, "dp", split_axis=1, concat_axis=0, tiled=True)
    pulled_rows, moved = lax.optimization_barrier((pulled_rows, moved))
    packed_of = dict(enumerate(moved))
    packed_of[last_section] = packed
    pulled_rows = pulled_rows.reshape(row_block_count, blocks_here, slot_count, width)
    own_counts = lax.dynamic_slice_in_dim(counts, dp_index * blocks_here, blocks_here)
    slot_valid = jnp.arange(slot_count, dtype=jnp.int32)[None, :] < own_counts[:, None]
    column_valid = jnp.repeat(slot_valid, row_block_count, axis=1)[:, None, :]
    query_row_items = queries.reshape(blocks_here, row_block_count, width)
    logits = (
        jnp.einsum(
            "ixp,wifp->ixfw", query_row_items, pulled_rows, preferred_element_type=jnp.float32
        )
        * INVERSE_TEMP
    )
    logits = logits.reshape(blocks_here, row_block_count, slot_count * row_block_count)
    target_logits = soft_weights(
        teacher.reshape(blocks_here, row_block_count, slot_count * row_block_count), column_valid
    )
    weight_matrices = (soft_weights(logits, column_valid) - target_logits).astype(jnp.bfloat16)
    weight_matrices = weight_matrices.reshape(
        blocks_here, row_block_count, slot_count, row_block_count
    )
    query_sums = (
        jnp.einsum(
            "geal,lgay->gey", weight_matrices, pulled_rows, preferred_element_type=jnp.float32
        )
        * INVERSE_TEMP
    )
    micro_count = section_inputs.shape[1] // dp_count
    micro_cols = jnp.transpose(
        query_sums[0, :micro_count].reshape(micro_count, dp_count, col_width), (1, 0, 2)
    )
    section_count = lax.axis_size("section")
    chunk = width // section_count
    term_pieces = (
        jnp.einsum(
            "fnydr,fnsc->sdryc",
            weight_matrices.reshape(blocks_here, row_block_count, slot_count, dp_count, stripe),
            query_row_items.reshape(blocks_here, row_block_count, section_count, chunk),
            preferred_element_type=jnp.float32,
        )
        * INVERSE_TEMP
    ).astype(jnp.bfloat16)
    term_pieces = term_pieces.reshape(section_count * dp_count, stripe, requests, chunk)
    own_slots = lax.dynamic_slice_in_dim(all_slots, dp_index * requests, requests)
    slot_tags = jnp.broadcast_to(
        own_slots.astype(jnp.bfloat16)[None, None, :, None],
        (section_count * dp_count, stripe, requests, 1),
    )
    term_pieces = jnp.concatenate([term_pieces, slot_tags], axis=3)
    entry = lax.all_to_all(micro_cols, "dp", split_axis=0, concat_axis=1, tiled=True)
    section_index = lax.axis_index("section")
    last = section_count - 1
    carry = entry.reshape(dp_count * micro_count, col_width)
    sent_of = {}
    for source in range(last, -1, -1):
        rows = packed_of[source][:col_width]
        pre = packed_of[source][col_width].astype(jnp.float32)
        sigma = jax.nn.sigmoid(pre)
        slope = sigma * (1.0 + pre * (1.0 - sigma))
        inner = (carry * slope).astype(jnp.bfloat16)
        piece = gathered_pieces(inner, "dp")
        back_sum = jnp.einsum("dmj,idj->mi", piece, rows, preferred_element_type=jnp.float32)
        carry = carry + back_sum
        if source == last:
            grad_cols, home_inner = carry, inner
        else:
            both = jnp.stack([carry, inner.astype(jnp.float32)])
            sent_of[source] = lax.ppermute(both, "section", [(last, source)])
    term_pieces, sent = lax.optimization_barrier(
        (term_pieces, tuple(sent_of[source] for source in range(last)))
    )
    for source in range(last):
        here = section_index == source
        grad_cols = jnp.where(here, sent[source][0], grad_cols)
        home_inner = jnp.where(here, sent[source][1].astype(jnp.bfloat16), home_inner)
    incoming_terms = lax.all_to_all(
        term_pieces, ("section", "dp"), split_axis=0, concat_axis=0, tiled=True
    )
    every_slot = incoming_terms[:, 0, :, chunk].astype(jnp.int32)
    onehot = (every_slot[:, :, None] == jnp.arange(block_total, dtype=jnp.int32)).astype(
        jnp.bfloat16
    )
    dense = jnp.einsum(
        "qsfc,qfn->snc",
        incoming_terms[:, :, :, :chunk],
        onehot,
        preferred_element_type=jnp.float32,
    )
    dense = dense.reshape(stripe, block_total, chunk).astype(jnp.bfloat16)
    passage_out = gathered_columns(dense.reshape(stripe * block_total, chunk), "section")
    passage_out = passage_out.reshape(stripe, block_total, width)
    home_piece = gathered_pieces(home_inner, "dp")
    grad_weight = (
        jnp.einsum("mi,dmj->idj", section_inputs[0], home_piece, preferred_element_type=jnp.float32)
        .reshape(col_width, width)
        .astype(jnp.bfloat16)
    )
    return (
        query_sums.reshape(blocks_here * row_block_count, width).astype(jnp.bfloat16),
        passage_out,
        grad_cols[None],
        grad_weight[None],
    )


def solution(mesh):
    placed = (
        P(("section", "dp"), None),
        P("dp", None, None),
        P("section", None),
        P("section"),
        P(("section", "dp"), None),
        P("section", "dp", None),
        P("section", None, "dp"),
        P("section", None, "dp"),
    )
    return jax.shard_map(
        body,
        mesh=mesh,
        in_specs=placed,
        out_specs=(
            P(("section", "dp"), None),
            P("dp", None, None),
            P("section", None, "dp"),
            P("section", "dp", None),
        ),
        check_vma=False,
    )
```

```python
import jax
import jax.numpy as jnp
from jax import lax
from jax.sharding import PartitionSpec as P

INVERSE_TEMP = 20.0


def passed_along(value, axis, steps):
    count = lax.axis_size(axis)
    initial, last = (max(0, -steps), min(count, count - steps))
    return lax.ppermute(value, axis, [(source, source + steps) for source in range(initial, last)])


def gathered_pieces(value, axis):
    count = lax.axis_size(axis)
    copies = jnp.broadcast_to(value[None], (count,) + value.shape)
    return lax.all_to_all(copies, axis, 0, 0, tiled=True)


def gathered_columns(value, axis):
    count = lax.axis_size(axis)
    copies = jnp.broadcast_to(value[None], (count,) + value.shape)
    pieces = lax.all_to_all(copies, axis, 0, 0, tiled=True)
    return jnp.transpose(pieces, (1, 0, 2)).reshape(value.shape[0], count * value.shape[1])


def soft_weights(logits, valid):
    masked = jnp.where(valid, logits, -1e30)
    highest = jnp.max(masked, axis=-1, keepdims=True)
    expons = jnp.where(valid, jnp.exp(masked - highest), 0.0)
    return expons / jnp.sum(expons, axis=-1, keepdims=True)


def body(queries, passages, candidates, counts, teacher, section_weights, section_inputs, pre_acts):
    dp_count = lax.axis_size("dp")
    dp_index = lax.axis_index("dp")
    stripe, block_total, width = passages.shape
    row_block_count = stripe * dp_count
    blocks_here = candidates.shape[0] // dp_count
    slot_count = candidates.shape[1]
    requests = blocks_here * slot_count
    all_slots = candidates.reshape(-1)
    chooser = (all_slots[:, None] == jnp.arange(block_total, dtype=jnp.int32)[None, :]).astype(
        passages.dtype
    )
    outgoing = jnp.einsum(
        "rpj,sp->rsj", passages, chooser, preferred_element_type=jnp.float32
    ).astype(passages.dtype)
    pulled_rows = lax.all_to_all(outgoing, "dp", split_axis=1, concat_axis=0, tiled=True)
    pulled_rows = pulled_rows.reshape(row_block_count, blocks_here, slot_count, width)
    own_counts = lax.dynamic_slice_in_dim(counts, dp_index * blocks_here, blocks_here)
    slot_valid = jnp.arange(slot_count, dtype=jnp.int32)[None, :] < own_counts[:, None]
    column_valid = jnp.repeat(slot_valid, row_block_count, axis=1)[:, None, :]
    query_row_items = queries.reshape(blocks_here, row_block_count, width)
    logits = (
        jnp.einsum(
            "ixp,wifp->ixfw", query_row_items, pulled_rows, preferred_element_type=jnp.float32
        )
        * INVERSE_TEMP
    )
    logits = logits.reshape(blocks_here, row_block_count, slot_count * row_block_count)
    target_logits = soft_weights(
        teacher.reshape(blocks_here, row_block_count, slot_count * row_block_count), column_valid
    )
    weight_matrices = (soft_weights(logits, column_valid) - target_logits).astype(jnp.bfloat16)
    weight_matrices = weight_matrices.reshape(
        blocks_here, row_block_count, slot_count, row_block_count
    )
    query_sums = (
        jnp.einsum(
            "geal,lgay->gey", weight_matrices, pulled_rows, preferred_element_type=jnp.float32
        )
        * INVERSE_TEMP
    )
    micro_count = section_inputs.shape[1] // dp_count
    col_width = width // dp_count
    micro_cols = jnp.transpose(
        query_sums[0, :micro_count].reshape(micro_count, dp_count, col_width), (1, 0, 2)
    )
    section_count = lax.axis_size("section")
    chunk = width // section_count
    term_pieces = (
        jnp.einsum(
            "fnydr,fnsc->sdryc",
            weight_matrices.reshape(blocks_here, row_block_count, slot_count, dp_count, stripe),
            query_row_items.reshape(blocks_here, row_block_count, section_count, chunk),
            preferred_element_type=jnp.float32,
        )
        * INVERSE_TEMP
    ).astype(jnp.bfloat16)
    term_pieces = term_pieces.reshape(section_count * dp_count, stripe, requests, chunk)
    own_slots = lax.dynamic_slice_in_dim(all_slots, dp_index * requests, requests)
    slot_tags = jnp.broadcast_to(
        own_slots.astype(jnp.bfloat16)[None, None, :, None],
        (section_count * dp_count, stripe, requests, 1),
    )
    term_pieces = jnp.concatenate([term_pieces, slot_tags], axis=3)
    incoming_terms = lax.all_to_all(
        term_pieces, ("section", "dp"), split_axis=0, concat_axis=0, tiled=True
    )
    incoming_terms, carry_start = lax.optimization_barrier((incoming_terms, micro_cols))
    every_slot = incoming_terms[:, 0, :, chunk].astype(jnp.int32)
    onehot = (every_slot[:, :, None] == jnp.arange(block_total, dtype=jnp.int32)).astype(
        jnp.bfloat16
    )
    dense = jnp.einsum(
        "qsfc,qfn->snc",
        incoming_terms[:, :, :, :chunk],
        onehot,
        preferred_element_type=jnp.float32,
    )
    dense = dense.reshape(stripe, block_total, chunk).astype(jnp.bfloat16)
    entry = lax.all_to_all(carry_start, "dp", split_axis=0, concat_axis=1, tiled=True)
    weight_rows = section_weights[0]
    split_rows = weight_rows.reshape(col_width, dp_count, col_width)
    input_cols = section_inputs[0]
    pre = pre_acts[0].astype(jnp.float32)
    sigma = jax.nn.sigmoid(pre)
    slope = sigma * (1.0 + pre * (1.0 - sigma))
    carry = entry.reshape(dp_count * micro_count, col_width)
    section_count = lax.axis_size("section")
    section_index = lax.axis_index("section")
    grad_cols = jnp.zeros_like(carry)
    grad_weight = jnp.zeros((col_width, width), jnp.float32)
    for section_turn in range(section_count):
        active_flag = section_count - 1 - section_turn
        inner = (carry * slope).astype(jnp.bfloat16)
        piece = gathered_pieces(inner, "dp")
        back_sum = jnp.einsum(
            "dmj,idj->mi", piece, split_rows, preferred_element_type=jnp.float32
        )
        weight_part = jnp.einsum(
            "mi,dmj->idj", input_cols, piece, preferred_element_type=jnp.float32
        ).reshape(col_width, width)
        back_sum, layer_weight = (back_sum, weight_part)
        updated = carry + back_sum
        is_active = section_index == active_flag
        grad_cols = jnp.where(is_active, updated, grad_cols)
        grad_weight = jnp.where(is_active, layer_weight, grad_weight)
        if section_turn + 1 < section_count:
            carry = passed_along(updated, "section", -1)
    dense, grad_cols = lax.optimization_barrier((dense, grad_cols))
    passage_out = gathered_columns(dense.reshape(stripe * block_total, chunk), "section")
    passage_out = passage_out.reshape(stripe, block_total, width)
    return (
        query_sums.reshape(blocks_here * row_block_count, width).astype(jnp.bfloat16),
        passage_out,
        grad_cols[None],
        grad_weight[None].astype(jnp.bfloat16),
    )


def solution(mesh):
    placed = (
        P(("section", "dp"), None),
        P("dp", None, None),
        P("section", None),
        P("section"),
        P(("section", "dp"), None),
        P("section", "dp", None),
        P("section", None, "dp"),
        P("section", None, "dp"),
    )
    return jax.shard_map(
        body,
        mesh=mesh,
        in_specs=placed,
        out_specs=(
            P(("section", "dp"), None),
            P("dp", None, None),
            P("section", None, "dp"),
            P("section", "dp", None),
        ),
        check_vma=False,
    )
```

```python
import jax
import jax.numpy as jnp
from jax import lax
from jax.sharding import PartitionSpec as P

INVERSE_TEMP = 20.0


def passed_along(value, axis, steps):
    count = lax.axis_size(axis)
    initial, last = (max(0, -steps), min(count, count - steps))
    return lax.ppermute(value, axis, [(source, source + steps) for source in range(initial, last)])


def gathered_pieces(value, axis):
    count = lax.axis_size(axis)
    copies = jnp.broadcast_to(value[None], (count,) + value.shape)
    return lax.all_to_all(copies, axis, 0, 0, tiled=True)


def gathered_columns(value, axis):
    count = lax.axis_size(axis)
    copies = jnp.broadcast_to(value[None], (count,) + value.shape)
    pieces = lax.all_to_all(copies, axis, 0, 0, tiled=True)
    return jnp.transpose(pieces, (1, 0, 2)).reshape(value.shape[0], count * value.shape[1])


def soft_weights(logits, valid):
    masked = jnp.where(valid, logits, -1e30)
    highest = jnp.max(masked, axis=-1, keepdims=True)
    expons = jnp.where(valid, jnp.exp(masked - highest), 0.0)
    return expons / jnp.sum(expons, axis=-1, keepdims=True)


def body(queries, passages, candidates, counts, teacher, section_weights, section_inputs, pre_acts):
    dp_count = lax.axis_size("dp")
    dp_index = lax.axis_index("dp")
    stripe, block_total, width = passages.shape
    row_block_count = stripe * dp_count
    blocks_here = candidates.shape[0] // dp_count
    slot_count = candidates.shape[1]
    requests = blocks_here * slot_count
    all_slots = candidates.reshape(-1)
    chooser = (all_slots[:, None] == jnp.arange(block_total, dtype=jnp.int32)[None, :]).astype(
        passages.dtype
    )
    outgoing = jnp.einsum(
        "rpj,sp->rsj", passages, chooser, preferred_element_type=jnp.float32
    ).astype(passages.dtype)
    pulled_rows = lax.all_to_all(outgoing, "dp", split_axis=1, concat_axis=0, tiled=True)
    pulled_rows = pulled_rows.reshape(row_block_count, blocks_here, slot_count, width)
    own_counts = lax.dynamic_slice_in_dim(counts, dp_index * blocks_here, blocks_here)
    slot_valid = jnp.arange(slot_count, dtype=jnp.int32)[None, :] < own_counts[:, None]
    column_valid = jnp.repeat(slot_valid, row_block_count, axis=1)[:, None, :]
    query_row_items = queries.reshape(blocks_here, row_block_count, width)
    logits = (
        jnp.einsum(
            "ixp,wifp->ixfw", query_row_items, pulled_rows, preferred_element_type=jnp.float32
        )
        * INVERSE_TEMP
    )
    logits = logits.reshape(blocks_here, row_block_count, slot_count * row_block_count)
    target_logits = soft_weights(
        teacher.reshape(blocks_here, row_block_count, slot_count * row_block_count), column_valid
    )
    weight_matrices = (soft_weights(logits, column_valid) - target_logits).astype(jnp.bfloat16)
    weight_matrices = weight_matrices.reshape(
        blocks_here, row_block_count, slot_count, row_block_count
    )
    query_sums = (
        jnp.einsum(
            "geal,lgay->gey", weight_matrices, pulled_rows, preferred_element_type=jnp.float32
        )
        * INVERSE_TEMP
    )
    micro_count = section_inputs.shape[1] // dp_count
    col_width = width // dp_count
    micro_cols = jnp.transpose(
        query_sums[0, :micro_count].reshape(micro_count, dp_count, col_width), (1, 0, 2)
    )
    section_count = lax.axis_size("section")
    chunk = width // section_count
    term_pieces = (
        jnp.einsum(
            "fnydr,fnsc->sdryc",
            weight_matrices.reshape(blocks_here, row_block_count, slot_count, dp_count, stripe),
            query_row_items.reshape(blocks_here, row_block_count, section_count, chunk),
            preferred_element_type=jnp.float32,
        )
        * INVERSE_TEMP
    ).astype(jnp.bfloat16)
    term_pieces = term_pieces.reshape(section_count * dp_count, stripe, requests, chunk)
    own_slots = lax.dynamic_slice_in_dim(all_slots, dp_index * requests, requests)
    slot_tags = jnp.broadcast_to(
        own_slots.astype(jnp.bfloat16)[None, None, :, None],
        (section_count * dp_count, stripe, requests, 1),
    )
    term_pieces = jnp.concatenate([term_pieces, slot_tags], axis=3)
    incoming_terms = lax.all_to_all(
        term_pieces, ("section", "dp"), split_axis=0, concat_axis=0, tiled=True
    )
    incoming_terms, carry_start = lax.optimization_barrier((incoming_terms, micro_cols))
    every_slot = incoming_terms[:, 0, :, chunk].astype(jnp.int32)
    onehot = (every_slot[:, :, None] == jnp.arange(block_total, dtype=jnp.int32)).astype(
        jnp.bfloat16
    )
    dense = jnp.einsum(
        "qsfc,qfn->snc",
        incoming_terms[:, :, :, :chunk],
        onehot,
        preferred_element_type=jnp.float32,
    )
    dense = dense.reshape(stripe, block_total, chunk).astype(jnp.bfloat16)
    passage_out = gathered_columns(dense.reshape(stripe * block_total, chunk), "section")
    passage_out = passage_out.reshape(stripe, block_total, width)
    entry = lax.all_to_all(carry_start, "dp", split_axis=0, concat_axis=1, tiled=True)
    weight_rows = section_weights[0]
    split_rows = weight_rows.reshape(col_width, dp_count, col_width)
    input_cols = section_inputs[0]
    pre = pre_acts[0].astype(jnp.float32)
    sigma = jax.nn.sigmoid(pre)
    slope = sigma * (1.0 + pre * (1.0 - sigma))
    carry = entry.reshape(dp_count * micro_count, col_width)
    section_count = lax.axis_size("section")
    section_index = lax.axis_index("section")
    grad_cols = jnp.zeros_like(carry)
    grad_weight = jnp.zeros((col_width, width), jnp.float32)
    for section_turn in range(section_count):
        active_flag = section_count - 1 - section_turn
        inner = (carry * slope).astype(jnp.bfloat16)
        piece = gathered_pieces(inner, "dp")
        back_sum = jnp.einsum(
            "dmj,idj->mi", piece, split_rows, preferred_element_type=jnp.float32
        )
        weight_part = jnp.einsum(
            "mi,dmj->idj", input_cols, piece, preferred_element_type=jnp.float32
        ).reshape(col_width, width)
        back_sum, layer_weight = (back_sum, weight_part)
        updated = carry + back_sum
        is_active = section_index == active_flag
        grad_cols = jnp.where(is_active, updated, grad_cols)
        grad_weight = jnp.where(is_active, layer_weight, grad_weight)
        if section_turn + 1 < section_count:
            carry = passed_along(updated, "section", -1)
    return (
        query_sums.reshape(blocks_here * row_block_count, width).astype(jnp.bfloat16),
        passage_out,
        grad_cols[None],
        grad_weight[None].astype(jnp.bfloat16),
    )


def solution(mesh):
    placed = (
        P(("section", "dp"), None),
        P("dp", None, None),
        P("section", None),
        P("section"),
        P(("section", "dp"), None),
        P("section", "dp", None),
        P("section", None, "dp"),
        P("section", None, "dp"),
    )
    return jax.shard_map(
        body,
        mesh=mesh,
        in_specs=placed,
        out_specs=(
            P(("section", "dp"), None),
            P("dp", None, None),
            P("section", None, "dp"),
            P("section", "dp", None),
        ),
        check_vma=False,
    )
```

```python
import jax
import jax.numpy as jnp
from jax import lax
from jax.sharding import PartitionSpec as P

INVERSE_TEMP = 20.0


def passed_along(value, axis, steps):
    count = lax.axis_size(axis)
    initial, last = (max(0, -steps), min(count, count - steps))
    return lax.ppermute(value, axis, [(source, source + steps) for source in range(initial, last)])


def gathered_pieces(value, axis):
    count = lax.axis_size(axis)
    copies = jnp.broadcast_to(value[None], (count,) + value.shape)
    return lax.all_to_all(copies, axis, 0, 0, tiled=True)


def soft_weights(logits, valid):
    masked = jnp.where(valid, logits, -1e30)
    highest = jnp.max(masked, axis=-1, keepdims=True)
    expons = jnp.where(valid, jnp.exp(masked - highest), 0.0)
    return expons / jnp.sum(expons, axis=-1, keepdims=True)


def body(queries, passages, candidates, counts, teacher, section_weights, section_inputs, pre_acts):
    dp_count = lax.axis_size("dp")
    dp_index = lax.axis_index("dp")
    stripe, block_total, width = passages.shape
    row_block_count = stripe * dp_count
    blocks_here = candidates.shape[0] // dp_count
    slot_count = candidates.shape[1]
    requests = blocks_here * slot_count
    all_slots = candidates.reshape(-1)
    chooser = (all_slots[:, None] == jnp.arange(block_total, dtype=jnp.int32)[None, :]).astype(
        passages.dtype
    )
    outgoing = jnp.einsum(
        "rpj,sp->rsj", passages, chooser, preferred_element_type=jnp.float32
    ).astype(passages.dtype)
    pulled_rows = lax.all_to_all(outgoing, "dp", split_axis=1, concat_axis=0, tiled=True)
    pulled_rows = pulled_rows.reshape(row_block_count, blocks_here, slot_count, width)
    own_counts = lax.dynamic_slice_in_dim(counts, dp_index * blocks_here, blocks_here)
    slot_valid = jnp.arange(slot_count, dtype=jnp.int32)[None, :] < own_counts[:, None]
    column_valid = jnp.repeat(slot_valid, row_block_count, axis=1)[:, None, :]
    query_row_items = queries.reshape(blocks_here, row_block_count, width)
    logits = (
        jnp.einsum(
            "ixp,wifp->ixfw", query_row_items, pulled_rows, preferred_element_type=jnp.float32
        )
        * INVERSE_TEMP
    )
    logits = logits.reshape(blocks_here, row_block_count, slot_count * row_block_count)
    target_logits = soft_weights(
        teacher.reshape(blocks_here, row_block_count, slot_count * row_block_count), column_valid
    )
    weight_matrices = (soft_weights(logits, column_valid) - target_logits).astype(jnp.bfloat16)
    weight_matrices = weight_matrices.reshape(
        blocks_here, row_block_count, slot_count, row_block_count
    )
    query_sums = (
        jnp.einsum(
            "geal,lgay->gey", weight_matrices, pulled_rows, preferred_element_type=jnp.float32
        )
        * INVERSE_TEMP
    )
    micro_count = section_inputs.shape[1] // dp_count
    col_width = width // dp_count
    micro_cols = jnp.transpose(
        query_sums[0, :micro_count].reshape(micro_count, dp_count, col_width), (1, 0, 2)
    )
    section_count = lax.axis_size("section")
    chunk = width // section_count
    term_pieces = (
        jnp.einsum(
            "fnydr,fnsc->sdryc",
            weight_matrices.reshape(blocks_here, row_block_count, slot_count, dp_count, stripe),
            query_row_items.reshape(blocks_here, row_block_count, section_count, chunk),
            preferred_element_type=jnp.float32,
        )
        * INVERSE_TEMP
    ).astype(jnp.bfloat16)
    term_pieces = term_pieces.reshape(section_count * dp_count, stripe, requests, chunk)
    own_slots = lax.dynamic_slice_in_dim(all_slots, dp_index * requests, requests)
    slot_tags = jnp.broadcast_to(
        own_slots.astype(jnp.bfloat16)[None, None, :, None],
        (section_count * dp_count, stripe, requests, 1),
    )
    term_pieces = jnp.concatenate([term_pieces, slot_tags], axis=3)
    incoming_terms = lax.all_to_all(
        term_pieces, ("section", "dp"), split_axis=0, concat_axis=0, tiled=True
    )
    incoming_terms, carry_start = lax.optimization_barrier((incoming_terms, micro_cols))
    every_slot = incoming_terms[:, 0, :, chunk].astype(jnp.int32)
    onehot = (every_slot[:, :, None] == jnp.arange(block_total, dtype=jnp.int32)).astype(
        jnp.bfloat16
    )
    dense = jnp.einsum(
        "qsfc,qfn->snc",
        incoming_terms[:, :, :, :chunk],
        onehot,
        preferred_element_type=jnp.float32,
    )
    dense = dense.reshape(stripe, block_total, chunk).astype(jnp.bfloat16)
    passage_out = lax.all_gather(dense, "section", axis=2, tiled=True)
    entry = lax.all_to_all(carry_start, "dp", split_axis=0, concat_axis=1, tiled=True)
    weight_rows = section_weights[0]
    split_rows = weight_rows.reshape(col_width, dp_count, col_width)
    input_cols = section_inputs[0]
    pre = pre_acts[0].astype(jnp.float32)
    sigma = jax.nn.sigmoid(pre)
    slope = sigma * (1.0 + pre * (1.0 - sigma))
    carry = entry.reshape(dp_count * micro_count, col_width)
    section_count = lax.axis_size("section")
    section_index = lax.axis_index("section")
    grad_cols = jnp.zeros_like(carry)
    grad_weight = jnp.zeros((col_width, width), jnp.float32)
    for section_turn in range(section_count):
        active_flag = section_count - 1 - section_turn
        inner = (carry * slope).astype(jnp.bfloat16)
        piece = gathered_pieces(inner, "dp")
        back_sum = jnp.einsum(
            "dmj,idj->mi", piece, split_rows, preferred_element_type=jnp.float32
        )
        weight_part = jnp.einsum(
            "mi,dmj->idj", input_cols, piece, preferred_element_type=jnp.float32
        ).reshape(col_width, width)
        back_sum, layer_weight = (back_sum, weight_part)
        updated = carry + back_sum
        is_active = section_index == active_flag
        grad_cols = jnp.where(is_active, updated, grad_cols)
        grad_weight = jnp.where(is_active, layer_weight, grad_weight)
        if section_turn + 1 < section_count:
            carry = passed_along(updated, "section", -1)
    return (
        query_sums.reshape(blocks_here * row_block_count, width).astype(jnp.bfloat16),
        passage_out,
        grad_cols[None],
        grad_weight[None].astype(jnp.bfloat16),
    )


def solution(mesh):
    placed = (
        P(("section", "dp"), None),
        P("dp", None, None),
        P("section", None),
        P("section"),
        P(("section", "dp"), None),
        P("section", "dp", None),
        P("section", None, "dp"),
        P("section", None, "dp"),
    )
    return jax.shard_map(
        body,
        mesh=mesh,
        in_specs=placed,
        out_specs=(
            P(("section", "dp"), None),
            P("dp", None, None),
            P("section", None, "dp"),
            P("section", "dp", None),
        ),
        check_vma=False,
    )
```

```python
import jax
import jax.numpy as jnp
from jax import lax
from jax.sharding import PartitionSpec as P

INVERSE_TEMP = 20.0


def passed_along(value, axis, steps):
    count = lax.axis_size(axis)
    initial, last = (max(0, -steps), min(count, count - steps))
    return lax.ppermute(value, axis, [(source, source + steps) for source in range(initial, last)])


def gathered_pieces(value, axis):
    count = lax.axis_size(axis)
    copies = jnp.broadcast_to(value[None], (count,) + value.shape)
    return lax.all_to_all(copies, axis, 0, 0, tiled=True)


def gathered_columns(value, axis):
    count = lax.axis_size(axis)
    copies = jnp.broadcast_to(value[None], (count,) + value.shape)
    pieces = lax.all_to_all(copies, axis, 0, 0, tiled=True)
    return jnp.transpose(pieces, (1, 0, 2)).reshape(value.shape[0], count * value.shape[1])


def soft_weights(logits, valid):
    masked = jnp.where(valid, logits, -1e30)
    highest = jnp.max(masked, axis=-1, keepdims=True)
    expons = jnp.where(valid, jnp.exp(masked - highest), 0.0)
    return expons / jnp.sum(expons, axis=-1, keepdims=True)


def body(queries, passages, candidates, counts, teacher, section_weights, section_inputs, pre_acts):
    dp_count = lax.axis_size("dp")
    dp_index = lax.axis_index("dp")
    stripe, block_total, width = passages.shape
    row_block_count = stripe * dp_count
    blocks_here = candidates.shape[0] // dp_count
    slot_count = candidates.shape[1]
    requests = blocks_here * slot_count
    all_slots = candidates.reshape(-1)
    chooser = (all_slots[:, None] == jnp.arange(block_total, dtype=jnp.int32)[None, :]).astype(
        passages.dtype
    )
    outgoing = jnp.einsum(
        "rpj,sp->rsj", passages, chooser, preferred_element_type=jnp.float32
    ).astype(passages.dtype)
    pulled_rows = lax.all_to_all(outgoing, "dp", split_axis=1, concat_axis=0, tiled=True)
    every_slot = lax.all_gather(candidates, "section", axis=0, tiled=True)
    pulled_rows, every_slot = lax.optimization_barrier((pulled_rows, every_slot))
    pulled_rows = pulled_rows.reshape(row_block_count, blocks_here, slot_count, width)
    own_counts = lax.dynamic_slice_in_dim(counts, dp_index * blocks_here, blocks_here)
    slot_valid = jnp.arange(slot_count, dtype=jnp.int32)[None, :] < own_counts[:, None]
    column_valid = jnp.repeat(slot_valid, row_block_count, axis=1)[:, None, :]
    query_row_items = queries.reshape(blocks_here, row_block_count, width)
    logits = (
        jnp.einsum(
            "ixp,wifp->ixfw", query_row_items, pulled_rows, preferred_element_type=jnp.float32
        )
        * INVERSE_TEMP
    )
    logits = logits.reshape(blocks_here, row_block_count, slot_count * row_block_count)
    target_logits = soft_weights(
        teacher.reshape(blocks_here, row_block_count, slot_count * row_block_count), column_valid
    )
    weight_matrices = (soft_weights(logits, column_valid) - target_logits).astype(jnp.bfloat16)
    weight_matrices = weight_matrices.reshape(
        blocks_here, row_block_count, slot_count, row_block_count
    )
    query_sums = (
        jnp.einsum(
            "geal,lgay->gey", weight_matrices, pulled_rows, preferred_element_type=jnp.float32
        )
        * INVERSE_TEMP
    )
    micro_count = section_inputs.shape[1] // dp_count
    col_width = width // dp_count
    micro_cols = jnp.transpose(
        query_sums[0, :micro_count].reshape(micro_count, dp_count, col_width), (1, 0, 2)
    )
    section_count = lax.axis_size("section")
    chunk = width // section_count
    term_pieces = (
        jnp.einsum(
            "fnydr,fnsc->sdryc",
            weight_matrices.reshape(blocks_here, row_block_count, slot_count, dp_count, stripe),
            query_row_items.reshape(blocks_here, row_block_count, section_count, chunk),
            preferred_element_type=jnp.float32,
        )
        * INVERSE_TEMP
    ).astype(jnp.bfloat16)
    term_pieces = term_pieces.reshape(section_count * dp_count, stripe, requests, chunk)
    incoming_terms = lax.all_to_all(
        term_pieces, ("section", "dp"), split_axis=0, concat_axis=0, tiled=True
    )
    incoming_terms, carry_start = lax.optimization_barrier((incoming_terms, micro_cols))
    onehot = (every_slot[:, :, None] == jnp.arange(block_total, dtype=jnp.int32)).astype(
        jnp.bfloat16
    )
    dense = jnp.einsum(
        "qsfc,qfn->snc",
        incoming_terms,
        onehot,
        preferred_element_type=jnp.float32,
    )
    dense = dense.reshape(stripe, block_total, chunk).astype(jnp.bfloat16)
    passage_out = gathered_columns(dense.reshape(stripe * block_total, chunk), "section")
    passage_out = passage_out.reshape(stripe, block_total, width)
    entry = lax.all_to_all(carry_start, "dp", split_axis=0, concat_axis=1, tiled=True)
    weight_rows = section_weights[0]
    split_rows = weight_rows.reshape(col_width, dp_count, col_width)
    input_cols = section_inputs[0]
    pre = pre_acts[0].astype(jnp.float32)
    sigma = jax.nn.sigmoid(pre)
    slope = sigma * (1.0 + pre * (1.0 - sigma))
    carry = entry.reshape(dp_count * micro_count, col_width)
    section_count = lax.axis_size("section")
    section_index = lax.axis_index("section")
    grad_cols = jnp.zeros_like(carry)
    grad_weight = jnp.zeros((col_width, width), jnp.float32)
    for section_turn in range(section_count):
        active_flag = section_count - 1 - section_turn
        inner = (carry * slope).astype(jnp.bfloat16)
        piece = gathered_pieces(inner, "dp")
        back_sum = jnp.einsum(
            "dmj,idj->mi", piece, split_rows, preferred_element_type=jnp.float32
        )
        weight_part = jnp.einsum(
            "mi,dmj->idj", input_cols, piece, preferred_element_type=jnp.float32
        ).reshape(col_width, width)
        back_sum, layer_weight = (back_sum, weight_part)
        updated = carry + back_sum
        is_active = section_index == active_flag
        grad_cols = jnp.where(is_active, updated, grad_cols)
        grad_weight = jnp.where(is_active, layer_weight, grad_weight)
        if section_turn + 1 < section_count:
            carry = passed_along(updated, "section", -1)
    return (
        query_sums.reshape(blocks_here * row_block_count, width).astype(jnp.bfloat16),
        passage_out,
        grad_cols[None],
        grad_weight[None].astype(jnp.bfloat16),
    )


def solution(mesh):
    placed = (
        P(("section", "dp"), None),
        P("dp", None, None),
        P("section", None),
        P("section"),
        P(("section", "dp"), None),
        P("section", "dp", None),
        P("section", None, "dp"),
        P("section", None, "dp"),
    )
    return jax.shard_map(
        body,
        mesh=mesh,
        in_specs=placed,
        out_specs=(
            P(("section", "dp"), None),
            P("dp", None, None),
            P("section", None, "dp"),
            P("section", "dp", None),
        ),
        check_vma=False,
    )
```

```python
import jax
import jax.numpy as jnp
from jax import lax
from jax.sharding import PartitionSpec as P

INVERSE_TEMP = 20.0


def passed_along(value, axis, steps):
    count = lax.axis_size(axis)
    initial, last = (max(0, -steps), min(count, count - steps))
    return lax.ppermute(value, axis, [(source, source + steps) for source in range(initial, last)])


def gathered_pieces(value, axis):
    count = lax.axis_size(axis)
    copies = jnp.broadcast_to(value[None], (count,) + value.shape)
    return lax.all_to_all(copies, axis, 0, 0, tiled=True)


def gathered_columns(value, axis):
    count = lax.axis_size(axis)
    copies = jnp.broadcast_to(value[None], (count,) + value.shape)
    pieces = lax.all_to_all(copies, axis, 0, 0, tiled=True)
    return jnp.transpose(pieces, (1, 0, 2)).reshape(value.shape[0], count * value.shape[1])


def soft_weights(logits, valid):
    masked = jnp.where(valid, logits, -1e30)
    highest = jnp.max(masked, axis=-1, keepdims=True)
    expons = jnp.where(valid, jnp.exp(masked - highest), 0.0)
    return expons / jnp.sum(expons, axis=-1, keepdims=True)


def body(queries, passages, candidates, counts, teacher, section_weights, section_inputs, pre_acts):
    dp_count = lax.axis_size("dp")
    dp_index = lax.axis_index("dp")
    stripe, block_total, width = passages.shape
    row_block_count = stripe * dp_count
    blocks_here = candidates.shape[0] // dp_count
    slot_count = candidates.shape[1]
    requests = blocks_here * slot_count
    all_slots = candidates.reshape(-1)
    chooser = (all_slots[:, None] == jnp.arange(block_total, dtype=jnp.int32)[None, :]).astype(
        passages.dtype
    )
    outgoing = jnp.einsum(
        "rpj,sp->rsj", passages, chooser, preferred_element_type=jnp.float32
    ).astype(passages.dtype)
    pulled_rows = lax.all_to_all(outgoing, "dp", split_axis=1, concat_axis=0, tiled=True)
    pulled_rows = pulled_rows.reshape(row_block_count, blocks_here, slot_count, width)
    own_counts = lax.dynamic_slice_in_dim(counts, dp_index * blocks_here, blocks_here)
    slot_valid = jnp.arange(slot_count, dtype=jnp.int32)[None, :] < own_counts[:, None]
    column_valid = jnp.repeat(slot_valid, row_block_count, axis=1)[:, None, :]
    query_row_items = queries.reshape(blocks_here, row_block_count, width)
    logits = (
        jnp.einsum(
            "ixp,wifp->ixfw", query_row_items, pulled_rows, preferred_element_type=jnp.float32
        )
        * INVERSE_TEMP
    )
    logits = logits.reshape(blocks_here, row_block_count, slot_count * row_block_count)
    target_logits = soft_weights(
        teacher.reshape(blocks_here, row_block_count, slot_count * row_block_count), column_valid
    )
    weight_matrices = (soft_weights(logits, column_valid) - target_logits).astype(jnp.bfloat16)
    weight_matrices = weight_matrices.reshape(
        blocks_here, row_block_count, slot_count, row_block_count
    )
    query_sums = (
        jnp.einsum(
            "geal,lgay->gey", weight_matrices, pulled_rows, preferred_element_type=jnp.float32
        )
        * INVERSE_TEMP
    )
    micro_count = section_inputs.shape[1] // dp_count
    col_width = width // dp_count
    micro_cols = jnp.transpose(
        query_sums[0, :micro_count].reshape(micro_count, dp_count, col_width), (1, 0, 2)
    )
    section_count = lax.axis_size("section")
    chunk = width // section_count
    term_pieces = (
        jnp.einsum(
            "fnydr,fnsc->sdryc",
            weight_matrices.reshape(blocks_here, row_block_count, slot_count, dp_count, stripe),
            query_row_items.reshape(blocks_here, row_block_count, section_count, chunk),
            preferred_element_type=jnp.float32,
        )
        * INVERSE_TEMP
    ).astype(jnp.bfloat16)
    term_pieces = term_pieces.reshape(section_count * dp_count, stripe, requests, chunk)
    own_slots = lax.dynamic_slice_in_dim(all_slots, dp_index * requests, requests)
    slot_tags = jnp.broadcast_to(
        own_slots.astype(jnp.bfloat16)[None, None, :, None],
        (section_count * dp_count, stripe, requests, 1),
    )
    term_pieces = jnp.concatenate([term_pieces, slot_tags], axis=3)
    incoming_terms = lax.all_to_all(
        term_pieces, ("section", "dp"), split_axis=0, concat_axis=0, tiled=True
    )
    every_slot = incoming_terms[:, 0, :, chunk].astype(jnp.int32)
    onehot = (every_slot[:, :, None] == jnp.arange(block_total, dtype=jnp.int32)).astype(
        jnp.bfloat16
    )
    dense = jnp.einsum(
        "qsfc,qfn->snc",
        incoming_terms[:, :, :, :chunk],
        onehot,
        preferred_element_type=jnp.float32,
    )
    dense = dense.reshape(stripe, block_total, chunk).astype(jnp.bfloat16)
    passage_out = gathered_columns(dense.reshape(stripe * block_total, chunk), "section")
    passage_out = passage_out.reshape(stripe, block_total, width)
    entry = lax.all_to_all(micro_cols, "dp", split_axis=0, concat_axis=1, tiled=True)
    weight_rows = section_weights[0]
    split_rows = weight_rows.reshape(col_width, dp_count, col_width)
    input_cols = section_inputs[0]
    pre = pre_acts[0].astype(jnp.float32)
    sigma = jax.nn.sigmoid(pre)
    slope = sigma * (1.0 + pre * (1.0 - sigma))
    carry = entry.reshape(dp_count * micro_count, col_width)
    section_count = lax.axis_size("section")
    section_index = lax.axis_index("section")
    grad_cols = jnp.zeros_like(carry)
    grad_weight = jnp.zeros((col_width, width), jnp.float32)
    for section_turn in range(section_count):
        active_flag = section_count - 1 - section_turn
        inner = (carry * slope).astype(jnp.bfloat16)
        piece = gathered_pieces(inner, "dp")
        back_sum = jnp.einsum(
            "dmj,idj->mi", piece, split_rows, preferred_element_type=jnp.float32
        )
        weight_part = jnp.einsum(
            "mi,dmj->idj", input_cols, piece, preferred_element_type=jnp.float32
        ).reshape(col_width, width)
        back_sum, layer_weight = (back_sum, weight_part)
        updated = carry + back_sum
        is_active = section_index == active_flag
        grad_cols = jnp.where(is_active, updated, grad_cols)
        grad_weight = jnp.where(is_active, layer_weight, grad_weight)
        if section_turn + 1 < section_count:
            carry = passed_along(updated, "section", -1)
    return (
        query_sums.reshape(blocks_here * row_block_count, width).astype(jnp.bfloat16),
        passage_out,
        grad_cols[None],
        grad_weight[None].astype(jnp.bfloat16),
    )


def solution(mesh):
    placed = (
        P(("section", "dp"), None),
        P("dp", None, None),
        P("section", None),
        P("section"),
        P(("section", "dp"), None),
        P("section", "dp", None),
        P("section", None, "dp"),
        P("section", None, "dp"),
    )
    return jax.shard_map(
        body,
        mesh=mesh,
        in_specs=placed,
        out_specs=(
            P(("section", "dp"), None),
            P("dp", None, None),
            P("section", None, "dp"),
            P("section", "dp", None),
        ),
        check_vma=False,
    )
```
